256 devices in a mesh: expert: 128 (over x, z, y), tensor: 2 (over core).
Axes of the slice: x: 4, y: 4, z: 8, core: 2. Of those that a mesh axis runs over, the one named last changes fastest.
Arguments:
- features: bfloat16 [16384, 3584], P('expert', 'tensor'), may hold values from -6 to 6
- cotangent: bfloat16 [16384, 3584], P('expert', 'tensor'), may hold values from -6 to 6
- expert_ids: int32 [16384, 2], P('expert'), may hold values from 0 to 127, all different within a row; in each aligned block of 128 rows (0 to 127, 128 to 255, ...) at most 3 rows name the same one
- route_weight: bfloat16 [16384, 2], P('expert'), may hold values from 0.099609375 to 1
- gate_weight: bfloat16 [128, 3584, 1024], P('expert', None, 'tensor'), may hold values from -0.09375 to 0.09375
- up_weight: bfloat16 [128, 3584, 1024], P('expert', None, 'tensor'), may hold values from -0.09375 to 0.09375
- down_weight: bfloat16 [128, 1024, 3584], P('expert', 'tensor'), may hold values from -0.1875 to 0.1875
Outputs:
- input_grad: bfloat16 [16384, 3584], P('expert', 'tensor')
The draws below stay inside these ranges and needn't reach their ends.
Inputs may be any that keep to these rules, and one draw needn't show every extreme that they name: `expert_ids`: each token names 2 different experts. Among the 128 tokens of one device (aligned blocks of rows) no expert is named by more than 3 tokens, a bound that some block reaches.
All inputs are finite; a program needn't handle non-finite values.
Results may differ from the reference program's by a relative error of at most 0.0058.
Values may be sent and summed in bfloat16 or wider, within the bound.
No kernel may reach another device: no remote copies, remote signals or barrier semaphores. Data moves between devices by JAX's collectives and lax.ppermute only.
A program may use at most 128 MiB of HBM per device.

```python
import math
import jax
import jax.numpy as jnp
import numpy as np
from jax import lax

D = 3584
FF = 1024
TOP = 2
TOK_DEV = 128
EXPERTS = 128
TOKENS = 16384
MOST = 3
N_EXPERT = 128


def level_of(stream_key, extent, split, low, high):
    factor_of = 1.0
    for axis_at, parts in split:
        steps = jax.random.uniform(jax.random.fold_in(jax.random.fold_in(stream_key, 6), axis_at), (parts,), jnp.float32, low / len(split), high / len(split))
        factor_of = factor_of * jnp.repeat(jnp.exp(steps), extent[axis_at] // parts).reshape((-1,) + (1,) * (len(extent) - 1 - axis_at))
    return factor_of


def routed_block(own_key, own, number, rows, amount, top, limit, lean):
    ranking = jax.random.permutation(own_key, amount)
    packed, usual = load_shares(amount, rows * top, limit, lean, True), load_shares(amount, rows * top, limit, lean, False)
    places = jnp.arange(amount)

    def named(tallies, rotation):
        used = int((tallies > 0).sum())
        fixed = max(1, used // 4)
        shifted = fixed + (places - fixed + rotation * (used - fixed)) % max(1, amount - fixed)
        return jnp.zeros((amount,), jnp.int32).at[ranking[jnp.where(places < fixed, places, shifted)]].set(jnp.asarray(tallies, jnp.int32))

    tallies = jnp.where(number % 4 == 0, named(packed, number // 4), named(usual, number - number // 4 - 1))
    mixed = jax.random.permutation(jax.random.fold_in(own, 3), amount)
    giver, taker = mixed[0:amount // 2 * 2:2], mixed[1:amount // 2 * 2:2]
    slack = jnp.minimum(tallies[giver] - 1, limit - tallies[taker]) // 2
    slack = jnp.where((giver == ranking[0]) | (taker == ranking[0]) | (tallies[taker] == 0), 0, jnp.maximum(slack, 0))
    shifted = jax.random.randint(jax.random.fold_in(own, 4), (amount // 2,), 0, 1 << 20) % (slack + 1)
    tallies = tallies.at[giver].add(-shifted).at[taker].add(shifted)
    items = jnp.searchsorted(jnp.cumsum(tallies), jnp.arange(rows * top), side="right").astype(jnp.int32)
    listing = items.reshape(top, rows).T
    listing = listing[jax.random.permutation(jax.random.fold_in(own, 1), rows)]
    rotation = jax.random.randint(jax.random.fold_in(own, 2), (rows, 1), 0, top)
    return jnp.take_along_axis(listing, (jnp.arange(top)[None, :] + rotation) % top, axis=1)


def load_shares(amount, total, bound, skew, full):
    portions = [(1 << 20) // math.isqrt(rank ** skew) + 1 for rank in range(1, amount + 1)]
    largest = bound if full else min(bound, max(-(-total // amount), total * portions[0] // sum(portions)))
    least = 1 if total - largest >= amount - 1 else 0
    counts, rest = [largest] + [least] * (amount - 1), total - largest - least * (amount - 1)
    while rest > 0:
        free = [i for i in range(1, amount) if counts[i] < largest] or [i for i in range(1, amount) if counts[i] < bound]
        pool, budget = sum([portions[i] for i in free]), rest
        for i in free:
            addition = min(bound - counts[i], max(1, budget * portions[i] // pool), rest)
            counts[i] = counts[i] + addition
            rest = rest - addition
    return np.array(counts)


def centred(rng, dims, width, limit, cuts=(), held_as=jnp.bfloat16):
    level = level_of(rng, dims, cuts, -0.22, 0.18) if cuts else 1.0
    result = jax.random.normal(rng, dims, jnp.float32) * width * level
    return jnp.minimum(jnp.maximum(result, -limit), limit).astype(held_as)


def setup_inputs(seed: int = 0) -> dict:
    key_list = jax.random.split(jax.random.key(seed), 8)
    features = centred(key_list[0], (TOKENS, D), 1.0, 6.0, ((0, 128), (1, 2)))
    cotangent = centred(key_list[1], (TOKENS, D), 1.0, 6.0, ((0, 128), (1, 2)))
    expert_ids_keys = jax.random.split(jax.random.fold_in(key_list[2], 1), TOKENS // TOK_DEV)
    expert_ids_turns = jax.random.permutation(jax.random.fold_in(key_list[2], 3), TOKENS // TOK_DEV)
    expert_ids = jax.vmap(lambda own, number: routed_block(jax.random.fold_in(key_list[2], 2), own, number, TOK_DEV, EXPERTS, TOP, MOST, 2))(expert_ids_keys, expert_ids_turns).reshape((TOKENS, TOP))
    route_weight = jnp.clip(0.099609375 + 0.9003906 * jax.random.uniform(key_list[3], (TOKENS, TOP), jnp.float32) ** level_of(key_list[3], (TOKENS, TOP), ((0, 128),), -0.2, 0.2), 0.099609375, 1.0).astype(jnp.bfloat16)
    gate_weight = centred(key_list[4], (EXPERTS, D, FF), D ** -0.5, 0.09375, ((0, 128), (2, 2)))
    up_weight = centred(key_list[5], (EXPERTS, D, FF), D ** -0.5, 0.09375, ((0, 128), (2, 2)))
    down_weight = centred(key_list[6], (EXPERTS, FF, D), FF ** -0.5, 0.1875, ((0, 128), (1, 2)))
    return dict(features=features, cotangent=cotangent, expert_ids=expert_ids, route_weight=route_weight, gate_weight=gate_weight, up_weight=up_weight, down_weight=down_weight)


def expert_rows(inputs, cotan_rows, weights, gate_w, up_w, down_w):
    gate_pre = jnp.dot(inputs, gate_w, preferred_element_type=jnp.float32)
    up_pre = jnp.dot(inputs, up_w, preferred_element_type=jnp.float32)
    hidden_grad = lax.dot_general(cotan_rows, down_w, (((1,), (1,)), ((), ())), preferred_element_type=jnp.float32)
    hidden_grad = hidden_grad * weights.astype(jnp.float32)[:, None]
    sigmoid_gate = jax.nn.sigmoid(gate_pre)
    gate_grad = (hidden_grad * up_pre * sigmoid_gate * (1.0 + gate_pre * (1.0 - sigmoid_gate))).astype(jnp.bfloat16)
    up_grad = (hidden_grad * gate_pre * sigmoid_gate).astype(jnp.bfloat16)
    first = lax.dot_general(gate_grad, gate_w, (((1,), (1,)), ((), ())), preferred_element_type=jnp.float32)
    second = lax.dot_general(up_grad, up_w, (((1,), (1,)), ((), ())), preferred_element_type=jnp.float32)
    return first + second


def reference(features, cotangent, expert_ids, route_weight, gate_weight, up_weight, down_weight):
    routes = TOKENS * TOP
    capacity = N_EXPERT * MOST
    flat_ids = expert_ids.reshape(routes).astype(jnp.int32)
    onehot = (flat_ids[:, None] == jnp.arange(EXPERTS, dtype=jnp.int32)[None, :]).astype(jnp.int32)
    ranks = jnp.sum((jnp.cumsum(onehot, axis=0) - 1) * onehot, axis=1).astype(jnp.int32)
    table = jnp.full((EXPERTS * capacity,), -1, jnp.int32)
    table = table.at[flat_ids * capacity + ranks].set(jnp.arange(routes, dtype=jnp.int32))
    table = table.reshape(EXPERTS, capacity)
    flat_weight = route_weight.reshape(routes)

    def one_expert(totals, inputs):
        column, gate_w, up_w, down_w = inputs
        filled = column >= 0
        source = jnp.maximum(column, 0).astype(jnp.int32)
        token_of = (source // TOP).astype(jnp.int32)
        rows_x = jnp.where(filled[:, None], features[token_of], jnp.zeros((), features.dtype))
        rows_dy = jnp.where(filled[:, None], cotangent[token_of], jnp.zeros((), cotangent.dtype))
        rows_w = jnp.where(filled, flat_weight[source], jnp.zeros((), flat_weight.dtype))
        grads = expert_rows(rows_x, rows_dy, rows_w, gate_w, up_w, down_w)
        rounded = lax.optimization_barrier(grads.astype(jnp.bfloat16)).astype(jnp.float32)
        rounded = jnp.where(filled[:, None], rounded, jnp.zeros((), jnp.float32))
        return totals.at[token_of].add(rounded), None

    totals, _ = lax.scan(one_expert, jnp.zeros((TOKENS, D), jnp.float32), (table, gate_weight, up_weight, down_weight))
    return totals.astype(jnp.bfloat16)
```

```python
import jax
import jax.numpy as jnp
from jax import lax
from jax.sharding import PartitionSpec as P


def expert_rows(xs, dys, weights, gate_w, up_w, down_w):
    parts, _, width = xs.shape
    ffh = gate_w.shape[1]
    gate_p = gate_w.reshape(parts, width, ffh)
    up_p = up_w.reshape(parts, width, ffh)
    down_p = down_w.reshape(ffh, parts, width)
    gate_pre = jnp.einsum("pnd,pdf->nf", xs, gate_p, preferred_element_type=jnp.float32)
    up_pre = jnp.einsum("pnd,pdf->nf", xs, up_p, preferred_element_type=jnp.float32)
    hidden_grad = jnp.einsum("pnd,fpd->nf", dys, down_p, preferred_element_type=jnp.float32)
    hidden_grad = hidden_grad * weights.astype(jnp.float32)[:, None]
    sigmoid_gate = jax.nn.sigmoid(gate_pre)
    gate_grad = (
        hidden_grad * up_pre * sigmoid_gate * (1.0 + gate_pre * (1.0 - sigmoid_gate))
    ).astype(jnp.bfloat16)
    up_grad = (hidden_grad * gate_pre * sigmoid_gate).astype(jnp.bfloat16)
    first = lax.dot_general(
        gate_grad, gate_w, (((1,), (1,)), ((), ())), preferred_element_type=jnp.float32
    )
    second = lax.dot_general(
        up_grad, up_w, (((1,), (1,)), ((), ())), preferred_element_type=jnp.float32
    )
    return first + second


def per_device(features, cotangent, expert_ids, route_weight, gate_weight, up_weight, down_weight):
    experts = lax.axis_size("expert")
    parts = lax.axis_size("tensor")
    tok_rows, top = expert_ids.shape
    half = features.shape[1]
    routes = tok_rows * top
    capacity = 3 * tok_rows * top // (2 * experts)
    total = experts * capacity
    flat_ids = expert_ids.reshape(routes)
    onehot = (flat_ids[:, None] == jnp.arange(experts, dtype=jnp.int32)[None, :]).astype(jnp.int32)
    ranks = jnp.sum((jnp.cumsum(onehot, axis=0) - 1) * onehot, axis=1)
    destination = flat_ids * capacity + ranks
    route_slot = destination[:, None] == jnp.arange(total, dtype=jnp.int32)[None, :]
    token_slot = jnp.sum(route_slot.reshape(tok_rows, top, total).astype(jnp.int32), axis=1)
    token_slot = token_slot.astype(jnp.bfloat16)
    slot_weight = jnp.sum(
        jnp.where(route_slot, route_weight.reshape(routes).astype(jnp.float32)[:, None], 0.0),
        axis=0,
    ).astype(jnp.bfloat16)

    token_rows = jnp.concatenate([features, cotangent], axis=1)
    packed = lax.dot_general(
        token_slot, token_rows, (((0,), (0,)), ((), ())), preferred_element_type=jnp.float32
    ).astype(jnp.bfloat16)
    lane = jnp.arange(128, dtype=jnp.int32)[None, :]
    weight_block = jnp.where(lane == 0, slot_weight[:, None], jnp.zeros((), jnp.bfloat16))
    outgoing = jnp.concatenate([packed, weight_block], axis=1)
    width = outgoing.shape[1]
    received = lax.all_to_all(
        outgoing.reshape(experts, capacity, width), "expert", split_axis=0, concat_axis=0, tiled=True
    ).reshape(total, width)
    both = lax.all_gather(received, "tensor", axis=0, tiled=False)
    xs = both[:, :, :half]
    dys = both[:, :, half : 2 * half]
    weights = received[:, 2 * half]
    partial_grad = expert_rows(xs, dys, weights, gate_weight[0], up_weight[0], down_weight[0])
    my_share = lax.psum_scatter(partial_grad, "tensor", scatter_dimension=1, tiled=True)
    back = my_share.astype(jnp.bfloat16).reshape(experts, capacity, half)
    returned = lax.all_to_all(back, "expert", split_axis=0, concat_axis=0, tiled=True)
    summed = jnp.dot(token_slot, returned.reshape(total, half), preferred_element_type=jnp.float32)
    return summed.astype(jnp.bfloat16)


def solution(mesh):
    in_specs = (
        P("expert", "tensor"),
        P("expert", "tensor"),
        P("expert", None),
        P("expert", None),
        P("expert", None, "tensor"),
        P("expert", None, "tensor"),
        P("expert", "tensor", None),
    )
    out_specs = P("expert", "tensor")
    return jax.shard_map(
        per_device, mesh=mesh, in_specs=in_specs, out_specs=out_specs, check_vma=False
    )
```

```python
import jax
import jax.numpy as jnp
from jax import lax
from jax.sharding import PartitionSpec as P


def fold_rows(rows, experts, lanes):
    per_expert = rows.size // experts
    return rows.reshape(experts, 4, per_expert // 4)


def per_device(features, cotangent, expert_ids, route_weight, gate_weight, up_weight, down_weight):
    experts = lax.axis_size("expert")
    parts = lax.axis_size("tensor")
    me = lax.axis_index("tensor")
    swap = [(i, (i + 1) % parts) for i in range(parts)]
    tok_rows, top = expert_ids.shape
    half = features.shape[1]
    routes = tok_rows * top
    capacity = 3 * tok_rows * top // (2 * experts)
    total = experts * capacity
    gate_w = gate_weight[0]
    up_w = up_weight[0]
    down_w = down_weight[0]
    ffh = gate_w.shape[1]

    other_rows = (me + 1) % parts * half
    sent_w = jnp.stack(
        [
            lax.dynamic_slice_in_dim(gate_w, other_rows, half, axis=0),
            lax.dynamic_slice_in_dim(up_w, other_rows, half, axis=0),
        ]
    )
    got_w = lax.ppermute(sent_w, "tensor", swap)
    own_gate = lax.dynamic_slice_in_dim(gate_w, me * half, half, axis=0)
    own_up = lax.dynamic_slice_in_dim(up_w, me * half, half, axis=0)

    flat_ids = expert_ids.reshape(routes)
    onehot = (flat_ids[:, None] == jnp.arange(experts, dtype=jnp.int32)[None, :]).astype(jnp.int32)
    ranks = jnp.sum((jnp.cumsum(onehot, axis=0) - 1) * onehot, axis=1)
    destination = flat_ids * capacity + ranks
    route_slot = destination[:, None] == jnp.arange(total, dtype=jnp.int32)[None, :]
    token_slot = jnp.sum(route_slot.reshape(tok_rows, top, total).astype(jnp.int32), axis=1)
    token_slot = token_slot.astype(jnp.bfloat16)
    slot_weight = jnp.sum(
        jnp.where(route_slot, route_weight.reshape(routes).astype(jnp.float32)[:, None], 0.0),
        axis=0,
    ).astype(jnp.bfloat16)

    token_rows = jnp.concatenate([features, cotangent], axis=1)
    packed = lax.dot_general(
        token_slot, token_rows, (((0,), (0,)), ((), ())), preferred_element_type=jnp.float32
    ).astype(jnp.bfloat16)
    row_part = fold_rows(packed, experts, 128)
    weight4 = jnp.pad(slot_weight.reshape(experts, capacity), ((0, 0), (0, 4 - capacity)))
    lane = jnp.arange(128, dtype=jnp.int32)[None, None, :]
    weight_part = jnp.where(lane == 0, weight4[:, :, None], jnp.zeros((), jnp.bfloat16))
    outgoing = jnp.concatenate([row_part, weight_part], axis=2)
    fold = row_part.shape[2]
    received = lax.all_to_all(outgoing, "expert", split_axis=0, concat_axis=0, tiled=True)
    weights = received[:, :capacity, fold].reshape(total)
    both = lax.all_gather(received, "tensor", axis=0, tiled=False)
    rows = both[:, :, :, :fold].reshape(parts, total, 2 * half)
    xs = rows[:, :, :half]
    dys = rows[:, :, half:]

    gate_pre = jnp.einsum(
        "pnd,pdf->nf", xs, gate_w.reshape(parts, half, ffh), preferred_element_type=jnp.float32
    )
    up_pre = jnp.einsum(
        "pnd,pdf->nf", xs, up_w.reshape(parts, half, ffh), preferred_element_type=jnp.float32
    )
    hidden_grad = None
    for p in range(parts):
        term = lax.dot_general(
            dys[p],
            lax.slice_in_dim(down_w, p * half, (p + 1) * half, axis=1),
            (((1,), (1,)), ((), ())),
            preferred_element_type=jnp.float32,
        )
        hidden_grad = term if hidden_grad is None else hidden_grad + term
    hidden_grad = hidden_grad * weights.astype(jnp.float32)[:, None]
    sigmoid_gate = jax.nn.sigmoid(gate_pre)
    gate_grad = (
        hidden_grad * up_pre * sigmoid_gate * (1.0 + gate_pre * (1.0 - sigmoid_gate))
    ).astype(jnp.bfloat16)
    up_grad = (hidden_grad * gate_pre * sigmoid_gate).astype(jnp.bfloat16)
    got_grad = lax.ppermute(jnp.concatenate([gate_grad, up_grad], axis=1), "tensor", swap)

    def back(grad, weight):
        return lax.dot_general(
            grad, weight, (((1,), (1,)), ((), ())), preferred_element_type=jnp.float32
        )

    share = (
        back(gate_grad, own_gate)
        + back(up_grad, own_up)
        + back(got_grad[:, :ffh], got_w[0])
        + back(got_grad[:, ffh:], got_w[1])
    )
    outgoing_back = fold_rows(share.astype(jnp.bfloat16), experts, 128)
    returned = lax.all_to_all(outgoing_back, "expert", split_axis=0, concat_axis=0, tiled=True)
    summed = jnp.dot(
        token_slot, returned.reshape(total, half), preferred_element_type=jnp.float32
    )
    return summed.astype(jnp.bfloat16)


def solution(mesh):
    in_specs = (
        P("expert", "tensor"),
        P("expert", "tensor"),
        P("expert", None),
        P("expert", None),
        P("expert", None, "tensor"),
        P("expert", None, "tensor"),
        P("expert", "tensor", None),
    )
    out_specs = P("expert", "tensor")
    return jax.shard_map(
        per_device, mesh=mesh, in_specs=in_specs, out_specs=out_specs, check_vma=False
    )
```

```python
import jax
import jax.numpy as jnp
from jax import lax
from jax.sharding import PartitionSpec as P


def fold_rows(rows, experts, lanes):
    per_expert = rows.size // experts
    return rows.reshape(experts, 4, per_expert // 4)


def per_device(features, cotangent, expert_ids, route_weight, gate_weight, up_weight, down_weight):
    experts = lax.axis_size("expert")
    parts = lax.axis_size("tensor")
    me = lax.axis_index("tensor")
    swap = [(i, (i + 1) % parts) for i in range(parts)]
    tok_rows, top = expert_ids.shape
    half = features.shape[1]
    routes = tok_rows * top
    capacity = 3 * tok_rows * top // (2 * experts)
    total = experts * capacity
    gate_w = gate_weight[0]
    up_w = up_weight[0]
    down_w = down_weight[0]
    ffh = gate_w.shape[1]

    other_rows = (me + 1) % parts * half
    sent_w = jnp.stack(
        [
            lax.dynamic_slice_in_dim(gate_w, other_rows, half, axis=0),
            lax.dynamic_slice_in_dim(up_w, other_rows, half, axis=0),
        ]
    )
    got_w = lax.ppermute(sent_w, "tensor", swap)
    own_gate = lax.dynamic_slice_in_dim(gate_w, me * half, half, axis=0)
    own_up = lax.dynamic_slice_in_dim(up_w, me * half, half, axis=0)

    flat_ids = expert_ids.reshape(routes)
    onehot = (flat_ids[:, None] == jnp.arange(experts, dtype=jnp.int32)[None, :]).astype(jnp.int32)
    ranks = jnp.sum((jnp.cumsum(onehot, axis=0) - 1) * onehot, axis=1)
    destination = flat_ids * capacity + ranks
    route_slot = destination[:, None] == jnp.arange(total, dtype=jnp.int32)[None, :]
    token_slot = jnp.sum(route_slot.reshape(tok_rows, top, total).astype(jnp.int32), axis=1)
    token_slot = token_slot.astype(jnp.bfloat16)
    slot_weight = jnp.sum(
        jnp.where(route_slot, route_weight.reshape(routes).astype(jnp.float32)[:, None], 0.0),
        axis=0,
    ).astype(jnp.bfloat16)

    token_rows = jnp.concatenate([features, cotangent], axis=1)
    packed = lax.dot_general(
        token_slot, token_rows, (((0,), (0,)), ((), ())), preferred_element_type=jnp.float32
    ).astype(jnp.bfloat16)
    row_part = fold_rows(packed, experts, 128)
    weight4 = jnp.pad(slot_weight.reshape(experts, capacity), ((0, 0), (0, 4 - capacity)))
    lane = jnp.arange(128, dtype=jnp.int32)[None, None, :]
    weight_part = jnp.where(lane == 0, weight4[:, :, None], jnp.zeros((), jnp.bfloat16))
    outgoing = jnp.concatenate([row_part, weight_part], axis=2)
    fold = row_part.shape[2]
    received = lax.all_to_all(outgoing, "expert", split_axis=0, concat_axis=0, tiled=True)
    weights = received[:, :capacity, fold].reshape(total)
    own_rows = received[:, :, :fold].reshape(total, 2 * half)
    got_rows = lax.ppermute(own_rows, "tensor", swap)
    other_cols = (me + 1) % parts * half
    own_down = lax.dynamic_slice_in_dim(down_w, me * half, half, axis=1)
    other_down = lax.dynamic_slice_in_dim(down_w, other_cols, half, axis=1)

    def fwd(rows, weight):
        return jnp.dot(rows, weight, preferred_element_type=jnp.float32)

    def fwd_t(rows, weight):
        return lax.dot_general(
            rows, weight, (((1,), (1,)), ((), ())), preferred_element_type=jnp.float32
        )

    gate_pre = fwd(own_rows[:, :half], own_gate) + fwd(got_rows[:, :half], sent_w[0])
    up_pre = fwd(own_rows[:, :half], own_up) + fwd(got_rows[:, :half], sent_w[1])
    hidden_grad = fwd_t(own_rows[:, half:], own_down) + fwd_t(got_rows[:, half:], other_down)
    hidden_grad = hidden_grad * weights.astype(jnp.float32)[:, None]
    sigmoid_gate = jax.nn.sigmoid(gate_pre)
    gate_grad = (
        hidden_grad * up_pre * sigmoid_gate * (1.0 + gate_pre * (1.0 - sigmoid_gate))
    ).astype(jnp.bfloat16)
    up_grad = (hidden_grad * gate_pre * sigmoid_gate).astype(jnp.bfloat16)
    got_grad = lax.ppermute(jnp.concatenate([gate_grad, up_grad], axis=1), "tensor", swap)

    def back(grad, weight):
        return lax.dot_general(
            grad, weight, (((1,), (1,)), ((), ())), preferred_element_type=jnp.float32
        )

    share = (
        back(gate_grad, own_gate)
        + back(up_grad, own_up)
        + back(got_grad[:, :ffh], got_w[0])
        + back(got_grad[:, ffh:], got_w[1])
    )
    outgoing_back = fold_rows(share.astype(jnp.bfloat16), experts, 128)
    returned = lax.all_to_all(outgoing_back, "expert", split_axis=0, concat_axis=0, tiled=True)
    summed = jnp.dot(
        token_slot, returned.reshape(total, half), preferred_element_type=jnp.float32
    )
    return summed.astype(jnp.bfloat16)


def solution(mesh):
    in_specs = (
        P("expert", "tensor"),
        P("expert", "tensor"),
        P("expert", None),
        P("expert", None),
        P("expert", None, "tensor"),
        P("expert", None, "tensor"),
        P("expert", "tensor", None),
    )
    out_specs = P("expert", "tensor")
    return jax.shard_map(
        per_device, mesh=mesh, in_specs=in_specs, out_specs=out_specs, check_vma=False
    )
```

```python
import jax
import jax.numpy as jnp
from jax import lax
from jax.sharding import PartitionSpec as P


def fold_rows(rows, experts):
    per_expert = rows.size // experts
    return rows.reshape(experts, 4, per_expert // 4)


def slot_ranks(ids, experts):
    onehot = (ids[:, None] == jnp.arange(experts, dtype=jnp.int32)[None, :]).astype(jnp.int32)
    return jnp.sum((jnp.cumsum(onehot, axis=0) - 1) * onehot, axis=1)


def device_body(features, cotangent, expert_ids, route_weight, gate_weight, up_weight, down_weight):
    experts = lax.axis_size("expert")
    parts = lax.axis_size("tensor")
    me = lax.axis_index("tensor")
    my_expert = lax.axis_index("expert")
    swap = [(i, (i + 1) % parts) for i in range(parts)]
    tok_rows, top = expert_ids.shape
    half = features.shape[1]
    routes = tok_rows * top
    capacity = 3 * tok_rows * top // (2 * experts)
    total = experts * capacity
    gate_w = gate_weight[0]
    up_w = up_weight[0]
    down_w = down_weight[0]

    coded = expert_ids * 4096 + (route_weight.astype(jnp.float32) * 2048.0).astype(jnp.int32)
    all_coded = lax.all_gather(coded, "expert", axis=0, tiled=True)
    all_coded = all_coded.reshape(experts, routes)
    all_ids = all_coded // 4096
    all_weights = (all_coded % 4096).astype(jnp.float32) * (1.0 / 2048.0)

    other_rows = (me + 1) % parts * half

    def rows_of(start):
        return jnp.concatenate(
            [
                lax.dynamic_slice_in_dim(gate_w, start, half, axis=0),
                lax.dynamic_slice_in_dim(up_w, start, half, axis=0),
            ],
            axis=1,
        )

    sent_gu = rows_of(other_rows)
    got_gu = lax.ppermute(sent_gu, "tensor", swap)
    own_gu = rows_of(me * half)

    flat_ids = expert_ids.reshape(routes)
    destination = flat_ids * capacity + slot_ranks(flat_ids, experts)
    route_slot = destination[:, None] == jnp.arange(total, dtype=jnp.int32)[None, :]
    token_slot = jnp.sum(route_slot.reshape(tok_rows, top, total).astype(jnp.int32), axis=1)
    token_slot = token_slot.astype(jnp.bfloat16)

    token_rows = jnp.concatenate([features, cotangent], axis=1)
    packed = lax.dot_general(
        token_slot, token_rows, (((0,), (0,)), ((), ())), preferred_element_type=jnp.float32
    ).astype(jnp.bfloat16)
    received = lax.all_to_all(
        fold_rows(packed, experts), "expert", split_axis=0, concat_axis=0, tiled=True
    )
    own_rows = received.reshape(total, 2 * half)
    got_rows = lax.ppermute(own_rows, "tensor", swap)

    mine = all_ids == my_expert
    rank = jnp.cumsum(mine.astype(jnp.int32), axis=1) - 1
    slot_of = jnp.where(mine, rank, capacity)
    weights = jnp.stack(
        [
            jnp.sum(jnp.where(slot_of == c, all_weights, 0.0), axis=1)
            for c in range(capacity)
        ],
        axis=1,
    ).reshape(total)

    other_cols = (me + 1) % parts * half
    own_down = lax.dynamic_slice_in_dim(down_w, me * half, half, axis=1)
    other_down = lax.dynamic_slice_in_dim(down_w, other_cols, half, axis=1)

    def fwd(rows, weight):
        return jnp.dot(rows, weight, preferred_element_type=jnp.float32)

    def fwd_t(rows, weight):
        return lax.dot_general(
            rows, weight, (((1,), (1,)), ((), ())), preferred_element_type=jnp.float32
        )

    ffh = gate_w.shape[1]
    gate_up = fwd(own_rows[:, :half], own_gu) + fwd(got_rows[:, :half], sent_gu)
    gate_pre = gate_up[:, :ffh]
    up_pre = gate_up[:, ffh:]
    hidden_grad = fwd_t(own_rows[:, half:], own_down) + fwd_t(got_rows[:, half:], other_down)
    hidden_grad = hidden_grad * weights[:, None]
    sigmoid_gate = jax.nn.sigmoid(gate_pre)
    gate_grad = (
        hidden_grad * up_pre * sigmoid_gate * (1.0 + gate_pre * (1.0 - sigmoid_gate))
    ).astype(jnp.bfloat16)
    up_grad = (hidden_grad * gate_pre * sigmoid_gate).astype(jnp.bfloat16)
    grads = jnp.concatenate([gate_grad, up_grad], axis=1)
    got_grads = lax.ppermute(grads, "tensor", swap)
    share = fwd_t(grads, own_gu) + fwd_t(got_grads, got_gu)
    returned = lax.all_to_all(
        fold_rows(share.astype(jnp.bfloat16), experts), "expert", split_axis=0, concat_axis=0, tiled=True
    )
    summed = jnp.dot(
        token_slot, returned.reshape(total, half), preferred_element_type=jnp.float32
    )
    return summed.astype(jnp.bfloat16)


def solution(mesh):
    in_specs = (
        P("expert", "tensor"),
        P("expert", "tensor"),
        P("expert", None),
        P("expert", None),
        P("expert", None, "tensor"),
        P("expert", None, "tensor"),
        P("expert", "tensor", None),
    )
    out_specs = P("expert", "tensor")
    return jax.shard_map(
        device_body, mesh=mesh, in_specs=in_specs, out_specs=out_specs, check_vma=False
    )
```

```python
import jax
import jax.numpy as jnp
from jax import lax
from jax.sharding import PartitionSpec as P


def fold_rows(rows, experts, lanes):
    per_expert = rows.size // experts
    return rows.reshape(experts, 4, per_expert // 4)


def per_device(features, cotangent, expert_ids, route_weight, gate_weight, up_weight, down_weight):
    experts = lax.axis_size("expert")
    parts = lax.axis_size("tensor")
    me = lax.axis_index("tensor")
    swap = [(i, (i + 1) % parts) for i in range(parts)]
    tok_rows, top = expert_ids.shape
    half = features.shape[1]
    routes = tok_rows * top
    capacity = 3 * tok_rows * top // (2 * experts)
    total = experts * capacity
    gate_w = gate_weight[0]
    up_w = up_weight[0]
    down_w = down_weight[0]
    ffh = gate_w.shape[1]

    other_rows = (me + 1) % parts * half

    def rows_of(start):
        return jnp.concatenate(
            [
                lax.dynamic_slice_in_dim(gate_w, start, half, axis=0),
                lax.dynamic_slice_in_dim(up_w, start, half, axis=0),
            ],
            axis=1,
        )

    sent_gu = rows_of(other_rows)
    got_gu = lax.ppermute(sent_gu, "tensor", swap)
    own_gu = rows_of(me * half)

    flat_ids = expert_ids.reshape(routes)
    onehot = (flat_ids[:, None] == jnp.arange(experts, dtype=jnp.int32)[None, :]).astype(jnp.int32)
    ranks = jnp.sum((jnp.cumsum(onehot, axis=0) - 1) * onehot, axis=1)
    destination = flat_ids * capacity + ranks
    route_slot = destination[:, None] == jnp.arange(total, dtype=jnp.int32)[None, :]
    token_slot = jnp.sum(route_slot.reshape(tok_rows, top, total).astype(jnp.int32), axis=1)
    token_slot = token_slot.astype(jnp.bfloat16)
    slot_weight = jnp.sum(
        jnp.where(route_slot, route_weight.reshape(routes).astype(jnp.float32)[:, None], 0.0),
        axis=0,
    ).astype(jnp.bfloat16)

    token_rows = jnp.concatenate([features, cotangent], axis=1)
    packed = lax.dot_general(
        token_slot, token_rows, (((0,), (0,)), ((), ())), preferred_element_type=jnp.float32
    ).astype(jnp.bfloat16)
    row_part = fold_rows(packed, experts, 128)
    weight4 = jnp.pad(slot_weight.reshape(experts, capacity), ((0, 0), (0, 4 - capacity)))
    lane = jnp.arange(128, dtype=jnp.int32)[None, None, :]
    weight_part = jnp.where(lane == 0, weight4[:, :, None], jnp.zeros((), jnp.bfloat16))
    outgoing = jnp.concatenate([row_part, weight_part], axis=2)
    fold = row_part.shape[2]
    received = lax.all_to_all(outgoing, "expert", split_axis=0, concat_axis=0, tiled=True)
    weights = received[:, :capacity, fold].reshape(total)
    own_rows = received[:, :, :fold].reshape(total, 2 * half)
    got_rows = lax.ppermute(own_rows, "tensor", swap)
    other_cols = (me + 1) % parts * half
    own_down = lax.dynamic_slice_in_dim(down_w, me * half, half, axis=1)
    other_down = lax.dynamic_slice_in_dim(down_w, other_cols, half, axis=1)

    def fwd(rows, weight):
        return jnp.dot(rows, weight, preferred_element_type=jnp.float32)

    def fwd_t(rows, weight):
        return lax.dot_general(
            rows, weight, (((1,), (1,)), ((), ())), preferred_element_type=jnp.float32
        )

    gate_up = fwd(own_rows[:, :half], own_gu) + fwd(got_rows[:, :half], sent_gu)
    gate_pre = gate_up[:, :ffh]
    up_pre = gate_up[:, ffh:]
    hidden_grad = fwd_t(own_rows[:, half:], own_down) + fwd_t(got_rows[:, half:], other_down)
    hidden_grad = hidden_grad * weights.astype(jnp.float32)[:, None]
    sigmoid_gate = jax.nn.sigmoid(gate_pre)
    gate_grad = (
        hidden_grad * up_pre * sigmoid_gate * (1.0 + gate_pre * (1.0 - sigmoid_gate))
    ).astype(jnp.bfloat16)
    up_grad = (hidden_grad * gate_pre * sigmoid_gate).astype(jnp.bfloat16)
    grads = jnp.concatenate([gate_grad, up_grad], axis=1)
    got_grads = lax.ppermute(grads, "tensor", swap)
    share = fwd_t(grads, own_gu) + fwd_t(got_grads, got_gu)
    outgoing_back = fold_rows(share.astype(jnp.bfloat16), experts, 128)
    returned = lax.all_to_all(outgoing_back, "expert", split_axis=0, concat_axis=0, tiled=True)
    summed = jnp.dot(
        token_slot, returned.reshape(total, half), preferred_element_type=jnp.float32
    )
    return summed.astype(jnp.bfloat16)


def solution(mesh):
    in_specs = (
        P("expert", "tensor"),
        P("expert", "tensor"),
        P("expert", None),
        P("expert", None),
        P("expert", None, "tensor"),
        P("expert", None, "tensor"),
        P("expert", "tensor", None),
    )
    out_specs = P("expert", "tensor")
    return jax.shard_map(
        per_device, mesh=mesh, in_specs=in_specs, out_specs=out_specs, check_vma=False
    )
```

```python
import jax
import jax.numpy as jnp
from jax import lax
from jax.sharding import PartitionSpec as P


def fold_rows(rows, experts, lanes):
    per_expert = rows.size // experts
    return rows.reshape(experts, 4, per_expert // 4)


def per_device(features, cotangent, expert_ids, route_weight, gate_weight, up_weight, down_weight):
    experts = lax.axis_size("expert")
    parts = lax.axis_size("tensor")
    me = lax.axis_index("tensor")
    swap = [(i, (i + 1) % parts) for i in range(parts)]
    tok_rows, top = expert_ids.shape
    half = features.shape[1]
    routes = tok_rows * top
    capacity = 3 * tok_rows * top // (2 * experts)
    total = experts * capacity
    gate_w = gate_weight[0]
    up_w = up_weight[0]
    down_w = down_weight[0]
    ffh = gate_w.shape[1]

    other_rows = (me + 1) % parts * half
    sent_w = jnp.stack(
        [
            lax.dynamic_slice_in_dim(gate_w, other_rows, half, axis=0),
            lax.dynamic_slice_in_dim(up_w, other_rows, half, axis=0),
        ]
    )
    got_w = lax.ppermute(sent_w, "tensor", swap)
    own_gate = lax.dynamic_slice_in_dim(gate_w, me * half, half, axis=0)
    own_up = lax.dynamic_slice_in_dim(up_w, me * half, half, axis=0)

    flat_ids = expert_ids.reshape(routes)
    onehot = (flat_ids[:, None] == jnp.arange(experts, dtype=jnp.int32)[None, :]).astype(jnp.int32)
    ranks = jnp.sum((jnp.cumsum(onehot, axis=0) - 1) * onehot, axis=1)
    destination = flat_ids * capacity + ranks
    route_slot = destination[:, None] == jnp.arange(total, dtype=jnp.int32)[None, :]
    token_slot = jnp.sum(route_slot.reshape(tok_rows, top, total).astype(jnp.int32), axis=1)
    token_slot = token_slot.astype(jnp.bfloat16)
    route_weight_slot = jnp.sum(
        jnp.where(route_slot, route_weight.reshape(routes).astype(jnp.float32)[:, None], 0.0)
        .reshape(tok_rows, top, total),
        axis=1,
    ).astype(jnp.bfloat16)

    token_rows = jnp.concatenate([features, cotangent], axis=1)
    packed = lax.dot_general(
        token_slot, token_rows, (((0,), (0,)), ((), ())), preferred_element_type=jnp.float32
    ).astype(jnp.bfloat16)
    received = lax.all_to_all(
        fold_rows(packed, experts, 128), "expert", split_axis=0, concat_axis=0, tiled=True
    )
    own_rows = received.reshape(total, 2 * half)
    got_rows = lax.ppermute(own_rows, "tensor", swap)
    other_cols = (me + 1) % parts * half
    own_down = lax.dynamic_slice_in_dim(down_w, me * half, half, axis=1)
    other_down = lax.dynamic_slice_in_dim(down_w, other_cols, half, axis=1)

    def fwd(rows, weight):
        return jnp.dot(rows, weight, preferred_element_type=jnp.float32)

    def fwd_t(rows, weight):
        return lax.dot_general(
            rows, weight, (((1,), (1,)), ((), ())), preferred_element_type=jnp.float32
        )

    gate_pre = fwd(own_rows[:, :half], own_gate) + fwd(got_rows[:, :half], sent_w[0])
    up_pre = fwd(own_rows[:, :half], own_up) + fwd(got_rows[:, :half], sent_w[1])
    hidden_grad = fwd_t(own_rows[:, half:], own_down) + fwd_t(got_rows[:, half:], other_down)
    sigmoid_gate = jax.nn.sigmoid(gate_pre)
    gate_grad = (
        hidden_grad * up_pre * sigmoid_gate * (1.0 + gate_pre * (1.0 - sigmoid_gate))
    ).astype(jnp.bfloat16)
    up_grad = (hidden_grad * gate_pre * sigmoid_gate).astype(jnp.bfloat16)
    got_grad = lax.ppermute(jnp.concatenate([gate_grad, up_grad], axis=1), "tensor", swap)

    def back(grad, weight):
        return lax.dot_general(
            grad, weight, (((1,), (1,)), ((), ())), preferred_element_type=jnp.float32
        )

    share = (
        back(gate_grad, own_gate)
        + back(up_grad, own_up)
        + back(got_grad[:, :ffh], got_w[0])
        + back(got_grad[:, ffh:], got_w[1])
    )
    outgoing_back = fold_rows(share.astype(jnp.bfloat16), experts, 128)
    returned = lax.all_to_all(outgoing_back, "expert", split_axis=0, concat_axis=0, tiled=True)
    summed = jnp.dot(
        route_weight_slot, returned.reshape(total, half), preferred_element_type=jnp.float32
    )
    return summed.astype(jnp.bfloat16)


def solution(mesh):
    in_specs = (
        P("expert", "tensor"),
        P("expert", "tensor"),
        P("expert", None),
        P("expert", None),
        P("expert", None, "tensor"),
        P("expert", None, "tensor"),
        P("expert", "tensor", None),
    )
    out_specs = P("expert", "tensor")
    return jax.shard_map(
        per_device, mesh=mesh, in_specs=in_specs, out_specs=out_specs, check_vma=False
    )
```

```python
import jax
import jax.numpy as jnp
from jax import lax
from jax.sharding import PartitionSpec as P


def fold_rows(rows, experts):
    per_expert = rows.size // experts
    return rows.reshape(experts, 4, per_expert // 4)


def device_body(features, cotangent, expert_ids, route_weight, gate_weight, up_weight, down_weight):
    experts = lax.axis_size("expert")
    parts = lax.axis_size("tensor")
    me = lax.axis_index("tensor")
    swap = [(i, (i + 1) % parts) for i in range(parts)]
    tok_rows, top = expert_ids.shape
    half = features.shape[1]
    routes = tok_rows * top
    capacity = 3 * tok_rows * top // (2 * experts)
    total = experts * capacity
    gate_w = gate_weight[0]
    up_w = up_weight[0]
    down_w = down_weight[0]
    ffh = gate_w.shape[1]

    other_rows = (me + 1) % parts * half
    sent_w = jnp.stack(
        [
            lax.dynamic_slice_in_dim(gate_w, other_rows, half, axis=0),
            lax.dynamic_slice_in_dim(up_w, other_rows, half, axis=0),
        ]
    )
    got_w = lax.ppermute(sent_w, "tensor", swap)
    own_gate = lax.dynamic_slice_in_dim(gate_w, me * half, half, axis=0)
    own_up = lax.dynamic_slice_in_dim(up_w, me * half, half, axis=0)

    flat_ids = expert_ids.reshape(routes)
    onehot = (flat_ids[:, None] == jnp.arange(experts, dtype=jnp.int32)[None, :]).astype(jnp.int32)
    ranks = jnp.sum((jnp.cumsum(onehot, axis=0) - 1) * onehot, axis=1)
    destination = flat_ids * capacity + ranks
    route_slot = destination[:, None] == jnp.arange(total, dtype=jnp.int32)[None, :]
    token_slot = jnp.sum(route_slot.reshape(tok_rows, top, total).astype(jnp.int32), axis=1)
    token_slot = token_slot.astype(jnp.bfloat16)
    route_weight_slot = jnp.sum(
        jnp.where(route_slot, route_weight.reshape(routes).astype(jnp.float32)[:, None], 0.0)
        .reshape(tok_rows, top, total),
        axis=1,
    ).astype(jnp.bfloat16)

    token_rows = jnp.concatenate([features, cotangent], axis=1)
    packed = lax.dot_general(
        token_slot, token_rows, (((0,), (0,)), ((), ())), preferred_element_type=jnp.float32
    ).astype(jnp.bfloat16)
    received = lax.all_to_all(
        fold_rows(packed, experts), "expert", split_axis=0, concat_axis=0, tiled=True
    )
    own_rows = received.reshape(total, 2 * half)
    got_rows = lax.ppermute(own_rows, "tensor", swap)
    other_cols = (me + 1) % parts * half
    own_down = lax.dynamic_slice_in_dim(down_w, me * half, half, axis=1)
    other_down = lax.dynamic_slice_in_dim(down_w, other_cols, half, axis=1)

    def fwd(rows, weight):
        return jnp.dot(rows, weight, preferred_element_type=jnp.float32)

    def fwd_t(rows, weight):
        return lax.dot_general(
            rows, weight, (((1,), (1,)), ((), ())), preferred_element_type=jnp.float32
        )

    gate_pre = fwd(own_rows[:, :half], own_gate) + fwd(got_rows[:, :half], sent_w[0])
    up_pre = fwd(own_rows[:, :half], own_up) + fwd(got_rows[:, :half], sent_w[1])
    hidden_grad = fwd_t(own_rows[:, half:], own_down) + fwd_t(got_rows[:, half:], other_down)
    sigmoid_gate = jax.nn.sigmoid(gate_pre)
    gate_grad = (
        hidden_grad * up_pre * sigmoid_gate * (1.0 + gate_pre * (1.0 - sigmoid_gate))
    ).astype(jnp.bfloat16)
    up_grad = (hidden_grad * gate_pre * sigmoid_gate).astype(jnp.bfloat16)
    got_grad = lax.ppermute(jnp.concatenate([gate_grad, up_grad], axis=1), "tensor", swap)

    def back(grad, weight):
        return lax.dot_general(
            grad, weight, (((1,), (1,)), ((), ())), preferred_element_type=jnp.float32
        )

    share = (
        back(gate_grad, own_gate)
        + back(up_grad, own_up)
        + back(got_grad[:, :ffh], got_w[0])
        + back(got_grad[:, ffh:], got_w[1])
    )
    outgoing_back = fold_rows(share.astype(jnp.bfloat16), experts)
    returned = lax.all_to_all(outgoing_back, "expert", split_axis=0, concat_axis=0, tiled=True)
    summed = jnp.dot(
        route_weight_slot, returned.reshape(total, half), preferred_element_type=jnp.float32
    )
    return summed.astype(jnp.bfloat16)


def solution(mesh):
    in_specs = (
        P("expert", "tensor"),
        P("expert", "tensor"),
        P("expert", None),
        P("expert", None),
        P("expert", None, "tensor"),
        P("expert", None, "tensor"),
        P("expert", "tensor", None),
    )
    out_specs = P("expert", "tensor")
    return jax.shard_map(
        device_body, mesh=mesh, in_specs=in_specs, out_specs=out_specs, check_vma=False
    )
```

```python
import jax
import jax.numpy as jnp
from jax import lax
from jax.sharding import PartitionSpec as P


def fold_rows(rows, experts):
    per_expert = rows.size // experts
    return rows.reshape(experts, 4, per_expert // 4)


def device_body(features, cotangent, expert_ids, route_weight, gate_weight, up_weight, down_weight):
    experts = lax.axis_size("expert")
    parts = lax.axis_size("tensor")
    me = lax.axis_index("tensor")
    swap = [(i, (i + 1) % parts) for i in range(parts)]
    tok_rows, top = expert_ids.shape
    half = features.shape[1]
    routes = tok_rows * top
    capacity = 3 * tok_rows * top // (2 * experts)
    total = experts * capacity
    gate_w = gate_weight[0]
    up_w = up_weight[0]
    down_w = down_weight[0]
    ffh = gate_w.shape[1]

    other_rows = (me + 1) % parts * half
    sent_w = jnp.stack(
        [
            lax.dynamic_slice_in_dim(gate_w, other_rows, half, axis=0),
            lax.dynamic_slice_in_dim(up_w, other_rows, half, axis=0),
        ]
    )
    got_w = lax.ppermute(sent_w, "tensor", swap)
    own_gate = lax.dynamic_slice_in_dim(gate_w, me * half, half, axis=0)
    own_up = lax.dynamic_slice_in_dim(up_w, me * half, half, axis=0)

    flat_ids = expert_ids.reshape(routes)
    onehot = (flat_ids[:, None] == jnp.arange(experts, dtype=jnp.int32)[None, :]).astype(jnp.int32)
    ranks = jnp.sum((jnp.cumsum(onehot, axis=0) - 1) * onehot, axis=1)
    destination = flat_ids * capacity + ranks
    route_slot = destination[:, None] == jnp.arange(total, dtype=jnp.int32)[None, :]
    token_slot = jnp.sum(route_slot.reshape(tok_rows, top, total).astype(jnp.int32), axis=1)
    token_slot = token_slot.astype(jnp.bfloat16)
    slot_weight = jnp.sum(
        jnp.where(route_slot, route_weight.reshape(routes).astype(jnp.float32)[:, None], 0.0),
        axis=0,
    ).astype(jnp.bfloat16)

    token_rows = jnp.concatenate([features, cotangent], axis=1)
    packed = lax.dot_general(
        token_slot, token_rows, (((0,), (0,)), ((), ())), preferred_element_type=jnp.float32
    ).astype(jnp.bfloat16)
    row_part = fold_rows(packed, experts)
    weight4 = jnp.pad(slot_weight.reshape(experts, capacity), ((0, 0), (0, 4 - capacity)))
    lane = jnp.arange(128, dtype=jnp.int32)[None, None, :]
    weight_part = jnp.where(lane == 0, weight4[:, :, None], jnp.zeros((), jnp.bfloat16))
    outgoing = jnp.concatenate([row_part, weight_part], axis=2)
    fold = row_part.shape[2]
    received = lax.all_to_all(outgoing, "expert", split_axis=0, concat_axis=0, tiled=True)
    weights = received[:, :capacity, fold].reshape(total)
    own_rows = received[:, :, :fold].reshape(total, 2 * half)
    got_rows = lax.ppermute(own_rows, "tensor", swap)
    other_cols = (me + 1) % parts * half
    own_down = lax.dynamic_slice_in_dim(down_w, me * half, half, axis=1)
    other_down = lax.dynamic_slice_in_dim(down_w, other_cols, half, axis=1)

    def fwd(rows, weight):
        return jnp.dot(rows, weight, preferred_element_type=jnp.float32)

    def fwd_t(rows, weight):
        return lax.dot_general(
            rows, weight, (((1,), (1,)), ((), ())), preferred_element_type=jnp.float32
        )

    gate_pre = fwd(own_rows[:, :half], own_gate) + fwd(got_rows[:, :half], sent_w[0])
    up_pre = fwd(own_rows[:, :half], own_up) + fwd(got_rows[:, :half], sent_w[1])
    hidden_grad = fwd_t(own_rows[:, half:], own_down) + fwd_t(got_rows[:, half:], other_down)
    hidden_grad = hidden_grad * weights.astype(jnp.float32)[:, None]
    sigmoid_gate = jax.nn.sigmoid(gate_pre)
    gate_grad = (
        hidden_grad * up_pre * sigmoid_gate * (1.0 + gate_pre * (1.0 - sigmoid_gate))
    ).astype(jnp.bfloat16)
    up_grad = (hidden_grad * gate_pre * sigmoid_gate).astype(jnp.bfloat16)
    got_grad = lax.ppermute(jnp.concatenate([gate_grad, up_grad], axis=1), "tensor", swap)

    def back(grad, weight):
        return lax.dot_general(
            grad, weight, (((1,), (1,)), ((), ())), preferred_element_type=jnp.float32
        )

    share = (
        back(gate_grad, own_gate)
        + back(up_grad, own_up)
        + back(got_grad[:, :ffh], got_w[0])
        + back(got_grad[:, ffh:], got_w[1])
    )
    outgoing_back = fold_rows(share.astype(jnp.bfloat16), experts)
    returned = lax.all_to_all(outgoing_back, "expert", split_axis=0, concat_axis=0, tiled=True)
    summed = jnp.dot(
        token_slot, returned.reshape(total, half), preferred_element_type=jnp.float32
    )
    return summed.astype(jnp.bfloat16)


def solution(mesh):
    in_specs = (
        P("expert", "tensor"),
        P("expert", "tensor"),
        P("expert", None),
        P("expert", None),
        P("expert", None, "tensor"),
        P("expert", None, "tensor"),
        P("expert", "tensor", None),
    )
    out_specs = P("expert", "tensor")
    return jax.shard_map(
        device_body, mesh=mesh, in_specs=in_specs, out_specs=out_specs, check_vma=False
    )
```

```python
import jax
import jax.numpy as jnp
from jax import lax
from jax.sharding import PartitionSpec as P


def fold_rows(rows, experts, folds):
    per_expert = rows.size // experts
    return rows.reshape(experts, folds, per_expert // folds)


def device_body(features, cotangent, expert_ids, route_weight, gate_weight, up_weight, down_weight):
    experts = lax.axis_size("expert")
    parts = lax.axis_size("tensor")
    me = lax.axis_index("tensor")
    swap = [(i, (i + 1) % parts) for i in range(parts)]
    tok_rows, top = expert_ids.shape
    half = features.shape[1]
    routes = tok_rows * top
    capacity = 3 * tok_rows * top // (2 * experts)
    total = experts * capacity
    gate_w = gate_weight[0]
    up_w = up_weight[0]
    down_w = down_weight[0]
    ffh = gate_w.shape[1]

    other_rows = (me + 1) % parts * half
    sent_w = jnp.stack(
        [
            lax.dynamic_slice_in_dim(gate_w, other_rows, half, axis=0),
            lax.dynamic_slice_in_dim(up_w, other_rows, half, axis=0),
        ]
    )
    got_w = lax.ppermute(sent_w, "tensor", swap)
    own_gate = lax.dynamic_slice_in_dim(gate_w, me * half, half, axis=0)
    own_up = lax.dynamic_slice_in_dim(up_w, me * half, half, axis=0)

    flat_ids = expert_ids.reshape(routes)
    onehot = (flat_ids[:, None] == jnp.arange(experts, dtype=jnp.int32)[None, :]).astype(jnp.int32)
    ranks = jnp.sum((jnp.cumsum(onehot, axis=0) - 1) * onehot, axis=1)
    destination = flat_ids * capacity + ranks
    route_slot = destination[:, None] == jnp.arange(total, dtype=jnp.int32)[None, :]
    token_slot = jnp.sum(route_slot.reshape(tok_rows, top, total).astype(jnp.int32), axis=1)
    token_slot = token_slot.astype(jnp.bfloat16)
    route_weight_slot = jnp.sum(
        jnp.where(route_slot, route_weight.reshape(routes).astype(jnp.float32)[:, None], 0.0)
        .reshape(tok_rows, top, total),
        axis=1,
    ).astype(jnp.bfloat16)

    token_rows = jnp.concatenate([features, cotangent], axis=1)
    packed = lax.dot_general(
        token_slot, token_rows, (((0,), (0,)), ((), ())), preferred_element_type=jnp.float32
    ).astype(jnp.bfloat16)
    received = lax.all_to_all(
        fold_rows(packed, experts, 4), "expert", split_axis=0, concat_axis=0, tiled=True
    )
    own_rows = received.reshape(total, 2 * half)
    got_rows = lax.ppermute(own_rows, "tensor", swap)
    other_cols = (me + 1) % parts * half
    own_down = lax.dynamic_slice_in_dim(down_w, me * half, half, axis=1)
    other_down = lax.dynamic_slice_in_dim(down_w, other_cols, half, axis=1)

    def fwd(rows, weight):
        return jnp.dot(rows, weight, preferred_element_type=jnp.float32)

    def fwd_t(rows, weight):
        return lax.dot_general(
            rows, weight, (((1,), (1,)), ((), ())), preferred_element_type=jnp.float32
        )

    gate_pre = fwd(own_rows[:, :half], own_gate) + fwd(got_rows[:, :half], sent_w[0])
    up_pre = fwd(own_rows[:, :half], own_up) + fwd(got_rows[:, :half], sent_w[1])
    hidden_grad = fwd_t(own_rows[:, half:], own_down) + fwd_t(got_rows[:, half:], other_down)
    sigmoid_gate = jax.nn.sigmoid(gate_pre)
    gate_grad = (
        hidden_grad * up_pre * sigmoid_gate * (1.0 + gate_pre * (1.0 - sigmoid_gate))
    ).astype(jnp.bfloat16)
    up_grad = (hidden_grad * gate_pre * sigmoid_gate).astype(jnp.bfloat16)
    got_grad = lax.ppermute(jnp.concatenate([gate_grad, up_grad], axis=1), "tensor", swap)

    def back(grad, weight):
        return lax.dot_general(
            grad, weight, (((1,), (1,)), ((), ())), preferred_element_type=jnp.float32
        )

    share = (
        back(gate_grad, own_gate)
        + back(up_grad, own_up)
        + back(got_grad[:, :ffh], got_w[0])
        + back(got_grad[:, ffh:], got_w[1])
    )
    outgoing_back = fold_rows(share.astype(jnp.bfloat16), experts, 2)
    returned = lax.all_to_all(outgoing_back, "expert", split_axis=0, concat_axis=0, tiled=True)
    summed = jnp.dot(
        route_weight_slot, returned.reshape(total, half), preferred_element_type=jnp.float32
    )
    return summed.astype(jnp.bfloat16)


def solution(mesh):
    in_specs = (
        P("expert", "tensor"),
        P("expert", "tensor"),
        P("expert", None),
        P("expert", None),
        P("expert", None, "tensor"),
        P("expert", None, "tensor"),
        P("expert", "tensor", None),
    )
    out_specs = P("expert", "tensor")
    return jax.shard_map(
        device_body, mesh=mesh, in_specs=in_specs, out_specs=out_specs, check_vma=False
    )
```

```python
import jax
import jax.numpy as jnp
from jax import lax
from jax.sharding import PartitionSpec as P


def fold_rows(rows, experts, folds):
    per_expert = rows.size // experts
    return rows.reshape(experts, folds, per_expert // folds)


def device_body(features, cotangent, expert_ids, route_weight, gate_weight, up_weight, down_weight):
    experts = lax.axis_size("expert")
    parts = lax.axis_size("tensor")
    me = lax.axis_index("tensor")
    swap = [(i, (i + 1) % parts) for i in range(parts)]
    tok_rows, top = expert_ids.shape
    half = features.shape[1]
    routes = tok_rows * top
    capacity = 3 * tok_rows * top // (2 * experts)
    total = experts * capacity
    gate_w = gate_weight[0]
    up_w = up_weight[0]
    down_w = down_weight[0]
    ffh = gate_w.shape[1]

    other_rows = (me + 1) % parts * half
    sent_w = jnp.stack(
        [
            lax.dynamic_slice_in_dim(gate_w, other_rows, half, axis=0),
            lax.dynamic_slice_in_dim(up_w, other_rows, half, axis=0),
        ]
    )
    got_w = lax.ppermute(sent_w, "tensor", swap)
    own_gate = lax.dynamic_slice_in_dim(gate_w, me * half, half, axis=0)
    own_up = lax.dynamic_slice_in_dim(up_w, me * half, half, axis=0)

    flat_ids = expert_ids.reshape(routes)
    onehot = (flat_ids[:, None] == jnp.arange(experts, dtype=jnp.int32)[None, :]).astype(jnp.int32)
    ranks = jnp.sum((jnp.cumsum(onehot, axis=0) - 1) * onehot, axis=1)
    destination = flat_ids * capacity + ranks
    route_slot = destination[:, None] == jnp.arange(total, dtype=jnp.int32)[None, :]
    token_slot = jnp.sum(route_slot.reshape(tok_rows, top, total).astype(jnp.int32), axis=1)
    token_slot = token_slot.astype(jnp.bfloat16)
    slot_weight = jnp.sum(
        jnp.where(route_slot, route_weight.reshape(routes).astype(jnp.float32)[:, None], 0.0),
        axis=0,
    ).astype(jnp.bfloat16)

    token_rows = jnp.concatenate([features, cotangent], axis=1)
    packed = lax.dot_general(
        token_slot, token_rows, (((0,), (0,)), ((), ())), preferred_element_type=jnp.float32
    ).astype(jnp.bfloat16)
    row_part = fold_rows(packed, experts, 4)
    weight4 = jnp.pad(slot_weight.reshape(experts, capacity), ((0, 0), (0, 4 - capacity)))
    lane = jnp.arange(128, dtype=jnp.int32)[None, None, :]
    weight_part = jnp.where(lane == 0, weight4[:, :, None], jnp.zeros((), jnp.bfloat16))
    outgoing = jnp.concatenate([row_part, weight_part], axis=2)
    fold = row_part.shape[2]
    received = lax.all_to_all(outgoing, "expert", split_axis=0, concat_axis=0, tiled=True)
    weights = received[:, :capacity, fold].reshape(total)
    own_rows = received[:, :, :fold].reshape(total, 2 * half)
    got_rows = lax.ppermute(own_rows, "tensor", swap)
    other_cols = (me + 1) % parts * half
    own_down = lax.dynamic_slice_in_dim(down_w, me * half, half, axis=1)
    other_down = lax.dynamic_slice_in_dim(down_w, other_cols, half, axis=1)

    def fwd(rows, weight):
        return jnp.dot(rows, weight, preferred_element_type=jnp.float32)

    def fwd_t(rows, weight):
        return lax.dot_general(
            rows, weight, (((1,), (1,)), ((), ())), preferred_element_type=jnp.float32
        )

    gate_pre = fwd(own_rows[:, :half], own_gate) + fwd(got_rows[:, :half], sent_w[0])
    up_pre = fwd(own_rows[:, :half], own_up) + fwd(got_rows[:, :half], sent_w[1])
    hidden_grad = fwd_t(own_rows[:, half:], own_down) + fwd_t(got_rows[:, half:], other_down)
    hidden_grad = hidden_grad * weights.astype(jnp.float32)[:, None]
    sigmoid_gate = jax.nn.sigmoid(gate_pre)
    gate_grad = (
        hidden_grad * up_pre * sigmoid_gate * (1.0 + gate_pre * (1.0 - sigmoid_gate))
    ).astype(jnp.bfloat16)
    up_grad = (hidden_grad * gate_pre * sigmoid_gate).astype(jnp.bfloat16)
    got_grad = lax.ppermute(jnp.concatenate([gate_grad, up_grad], axis=1), "tensor", swap)

    def back(grad, weight):
        return lax.dot_general(
            grad, weight, (((1,), (1,)), ((), ())), preferred_element_type=jnp.float32
        )

    share = (
        back(gate_grad, own_gate)
        + back(up_grad, own_up)
        + back(got_grad[:, :ffh], got_w[0])
        + back(got_grad[:, ffh:], got_w[1])
    )
    outgoing_back = fold_rows(share.astype(jnp.bfloat16), experts, 2)
    returned = lax.all_to_all(outgoing_back, "expert", split_axis=0, concat_axis=0, tiled=True)
    summed = jnp.dot(
        token_slot, returned.reshape(total, half), preferred_element_type=jnp.float32
    )
    return summed.astype(jnp.bfloat16)


def solution(mesh):
    in_specs = (
        P("expert", "tensor"),
        P("expert", "tensor"),
        P("expert", None),
        P("expert", None),
        P("expert", None, "tensor"),
        P("expert", None, "tensor"),
        P("expert", "tensor", None),
    )
    out_specs = P("expert", "tensor")
    return jax.shard_map(
        device_body, mesh=mesh, in_specs=in_specs, out_specs=out_specs, check_vma=False
    )
```

```python
import jax
import jax.numpy as jnp
from jax import lax
from jax.sharding import PartitionSpec as P


def fold_rows(rows, experts, folds):
    per_expert = rows.size // experts
    return rows.reshape(experts, folds, per_expert // folds)


def device_body(features, cotangent, expert_ids, route_weight, gate_weight, up_weight, down_weight):
    experts = lax.axis_size("expert")
    parts = lax.axis_size("tensor")
    me = lax.axis_index("tensor")
    swap = [(i, (i + 1) % parts) for i in range(parts)]
    tok_rows, top = expert_ids.shape
    half = features.shape[1]
    routes = tok_rows * top
    capacity = 3 * tok_rows * top // (2 * experts)
    total = experts * capacity
    gate_w = gate_weight[0]
    up_w = up_weight[0]
    down_w = down_weight[0]
    ffh = gate_w.shape[1]

    other_rows = (me + 1) % parts * half

    def rows_of(start):
        return jnp.concatenate(
            [
                lax.dynamic_slice_in_dim(gate_w, start, half, axis=0),
                lax.dynamic_slice_in_dim(up_w, start, half, axis=0),
            ],
            axis=1,
        )

    sent_gu = rows_of(other_rows)
    got_gu = lax.ppermute(sent_gu, "tensor", swap)
    own_gu = rows_of(me * half)

    flat_ids = expert_ids.reshape(routes)
    onehot = (flat_ids[:, None] == jnp.arange(experts, dtype=jnp.int32)[None, :]).astype(jnp.int32)
    ranks = jnp.sum((jnp.cumsum(onehot, axis=0) - 1) * onehot, axis=1)
    destination = flat_ids * capacity + ranks
    route_slot = destination[:, None] == jnp.arange(total, dtype=jnp.int32)[None, :]
    token_slot = jnp.sum(route_slot.reshape(tok_rows, top, total).astype(jnp.int32), axis=1)
    token_slot = token_slot.astype(jnp.bfloat16)
    route_weight_slot = jnp.sum(
        jnp.where(route_slot, route_weight.reshape(routes).astype(jnp.float32)[:, None], 0.0)
        .reshape(tok_rows, top, total),
        axis=1,
    ).astype(jnp.bfloat16)

    token_rows = jnp.concatenate([features, cotangent], axis=1)
    packed = lax.dot_general(
        token_slot, token_rows, (((0,), (0,)), ((), ())), preferred_element_type=jnp.float32
    ).astype(jnp.bfloat16)
    received = lax.all_to_all(
        fold_rows(packed, experts, 4), "expert", split_axis=0, concat_axis=0, tiled=True
    )
    own_rows = received.reshape(total, 2 * half)
    got_rows = lax.ppermute(own_rows, "tensor", swap)
    other_cols = (me + 1) % parts * half
    own_down = lax.dynamic_slice_in_dim(down_w, me * half, half, axis=1)
    other_down = lax.dynamic_slice_in_dim(down_w, other_cols, half, axis=1)

    def fwd(rows, weight):
        return jnp.dot(rows, weight, preferred_element_type=jnp.float32)

    def fwd_t(rows, weight):
        return lax.dot_general(
            rows, weight, (((1,), (1,)), ((), ())), preferred_element_type=jnp.float32
        )

    gate_up = fwd(own_rows[:, :half], own_gu) + fwd(got_rows[:, :half], sent_gu)
    gate_pre = gate_up[:, :ffh]
    up_pre = gate_up[:, ffh:]
    hidden_grad = fwd_t(own_rows[:, half:], own_down) + fwd_t(got_rows[:, half:], other_down)
    sigmoid_gate = jax.nn.sigmoid(gate_pre)
    gate_grad = (
        hidden_grad * up_pre * sigmoid_gate * (1.0 + gate_pre * (1.0 - sigmoid_gate))
    ).astype(jnp.bfloat16)
    up_grad = (hidden_grad * gate_pre * sigmoid_gate).astype(jnp.bfloat16)
    grads = jnp.concatenate([gate_grad, up_grad], axis=1)
    got_grads = lax.ppermute(grads, "tensor", swap)
    share = fwd_t(grads, own_gu) + fwd_t(got_grads, got_gu)
    outgoing_back = fold_rows(share.astype(jnp.bfloat16), experts, 2)
    returned = lax.all_to_all(outgoing_back, "expert", split_axis=0, concat_axis=0, tiled=True)
    summed = jnp.dot(
        route_weight_slot, returned.reshape(total, half), preferred_element_type=jnp.float32
    )
    return summed.astype(jnp.bfloat16)


def solution(mesh):
    in_specs = (
        P("expert", "tensor"),
        P("expert", "tensor"),
        P("expert", None),
        P("expert", None),
        P("expert", None, "tensor"),
        P("expert", None, "tensor"),
        P("expert", "tensor", None),
    )
    out_specs = P("expert", "tensor")
    return jax.shard_map(
        device_body, mesh=mesh, in_specs=in_specs, out_specs=out_specs, check_vma=False
    )
```

```python
import jax
import jax.numpy as jnp
from jax import lax
from jax.sharding import PartitionSpec as P


def fold_rows(rows, experts, folds):
    per_expert = rows.size // experts
    return rows.reshape(experts, folds, per_expert // folds)


def device_body(features, cotangent, expert_ids, route_weight, gate_weight, up_weight, down_weight):
    experts = lax.axis_size("expert")
    parts = lax.axis_size("tensor")
    me = lax.axis_index("tensor")
    swap = [(i, (i + 1) % parts) for i in range(parts)]
    tok_rows, top = expert_ids.shape
    half = features.shape[1]
    routes = tok_rows * top
    capacity = 3 * tok_rows * top // (2 * experts)
    total = experts * capacity
    gate_w = gate_weight[0]
    up_w = up_weight[0]
    down_w = down_weight[0]
    ffh = gate_w.shape[1]

    other_rows = (me + 1) % parts * half

    def rows_of(start):
        return jnp.concatenate(
            [
                lax.dynamic_slice_in_dim(gate_w, start, half, axis=0),
                lax.dynamic_slice_in_dim(up_w, start, half, axis=0),
            ],
            axis=1,
        )

    sent_gu = rows_of(other_rows)
    got_gu = lax.ppermute(sent_gu, "tensor", swap)
    own_gu = rows_of(me * half)

    flat_ids = expert_ids.reshape(routes)
    onehot = (flat_ids[:, None] == jnp.arange(experts, dtype=jnp.int32)[None, :]).astype(jnp.int32)
    ranks = jnp.sum((jnp.cumsum(onehot, axis=0) - 1) * onehot, axis=1)
    destination = flat_ids * capacity + ranks
    route_slot = destination[:, None] == jnp.arange(total, dtype=jnp.int32)[None, :]
    token_slot = jnp.sum(route_slot.reshape(tok_rows, top, total).astype(jnp.int32), axis=1)
    token_slot = token_slot.astype(jnp.bfloat16)
    slot_weight = jnp.sum(
        jnp.where(route_slot, route_weight.reshape(routes).astype(jnp.float32)[:, None], 0.0),
        axis=0,
    ).astype(jnp.bfloat16)

    token_rows = jnp.concatenate([features, cotangent], axis=1)
    packed = lax.dot_general(
        token_slot, token_rows, (((0,), (0,)), ((), ())), preferred_element_type=jnp.float32
    ).astype(jnp.bfloat16)
    row_part = fold_rows(packed, experts, 4)
    weight4 = jnp.pad(slot_weight.reshape(experts, capacity), ((0, 0), (0, 4 - capacity)))
    lane = jnp.arange(128, dtype=jnp.int32)[None, None, :]
    weight_part = jnp.where(lane == 0, weight4[:, :, None], jnp.zeros((), jnp.bfloat16))
    outgoing = jnp.concatenate([row_part, weight_part], axis=2)
    fold = row_part.shape[2]
    received = lax.all_to_all(outgoing, "expert", split_axis=0, concat_axis=0, tiled=True)
    weights = received[:, :capacity, fold].reshape(total)
    own_rows = received[:, :, :fold].reshape(total, 2 * half)
    got_rows = lax.ppermute(own_rows, "tensor", swap)
    other_cols = (me + 1) % parts * half
    own_down = lax.dynamic_slice_in_dim(down_w, me * half, half, axis=1)
    other_down = lax.dynamic_slice_in_dim(down_w, other_cols, half, axis=1)

    def fwd(rows, weight):
        return jnp.dot(rows, weight, preferred_element_type=jnp.float32)

    def fwd_t(rows, weight):
        return lax.dot_general(
            rows, weight, (((1,), (1,)), ((), ())), preferred_element_type=jnp.float32
        )

    gate_up = fwd(own_rows[:, :half], own_gu) + fwd(got_rows[:, :half], sent_gu)
    gate_pre = gate_up[:, :ffh]
    up_pre = gate_up[:, ffh:]
    hidden_grad = fwd_t(own_rows[:, half:], own_down) + fwd_t(got_rows[:, half:], other_down)
    hidden_grad = hidden_grad * weights.astype(jnp.float32)[:, None]
    sigmoid_gate = jax.nn.sigmoid(gate_pre)
    gate_grad = (
        hidden_grad * up_pre * sigmoid_gate * (1.0 + gate_pre * (1.0 - sigmoid_gate))
    ).astype(jnp.bfloat16)
    up_grad = (hidden_grad * gate_pre * sigmoid_gate).astype(jnp.bfloat16)
    grads = jnp.concatenate([gate_grad, up_grad], axis=1)
    got_grads = lax.ppermute(grads, "tensor", swap)
    share = fwd_t(grads, own_gu) + fwd_t(got_grads, got_gu)
    outgoing_back = fold_rows(share.astype(jnp.bfloat16), experts, 2)
    returned = lax.all_to_all(outgoing_back, "expert", split_axis=0, concat_axis=0, tiled=True)
    summed = jnp.dot(
        token_slot, returned.reshape(total, half), preferred_element_type=jnp.float32
    )
    return summed.astype(jnp.bfloat16)


def solution(mesh):
    in_specs = (
        P("expert", "tensor"),
        P("expert", "tensor"),
        P("expert", None),
        P("expert", None),
        P("expert", None, "tensor"),
        P("expert", None, "tensor"),
        P("expert", "tensor", None),
    )
    out_specs = P("expert", "tensor")
    return jax.shard_map(
        device_body, mesh=mesh, in_specs=in_specs, out_specs=out_specs, check_vma=False
    )
```
